512 devices in a mesh: attn: 64 (over y, z), dp: 4 (over x), tensor: 2 (over core).
Axes of the slice: x: 4, y: 4, z: 16, core: 2. Of those that a mesh axis runs over, the one named last changes fastest.
Arguments:
- hidden_state: bfloat16 [256, 8192], P('dp', 'attn'), may hold values from -6 to 6
- w_query: bfloat16 [8192, 8192], P('attn', 'tensor'), may hold values from -0.0625 to 0.0625
- w_keyval: bfloat16 [8192, 2, 1024], P('attn', None, 'tensor'), may hold values from -0.0625 to 0.0625
- w_output: bfloat16 [8192, 8192], P('tensor', 'attn'), may hold values from -0.0625 to 0.0625
- kv_cache: bfloat16 [4, 49152, 2, 8, 128], P('dp', 'attn', None, 'tensor'), as said below
- lengths: int32 [4, 64], P('dp'), may hold values from 1 to 256, 8192 in all within a row
- owner_of: int32 [4, 64, 1], P('dp'), may hold values from 0 to 63; in each aligned block of 64 rows (0 to 63, 64 to 127, ..., all dimensions but the last counted through in order) at most 3 rows name the same one
Outputs:
- attended: bfloat16 [256, 8192], P('dp', 'attn')
The draws below stay inside these ranges and needn't reach their ends.
Inputs may be any that keep to these rules, and one draw needn't show every extreme that they name: `owner_of`: in each data group at most 3 requests are placed on one attention device, and in some groups exactly 3 on one. The lengths of each data group sum to 8192, and the longest is exactly 256. `kv_cache`: finite keys and values.
All inputs are finite; a program needn't handle non-finite values.
Results may differ from the reference program's by a relative error of at most 0.009.
The reference program's roundings to bfloat16 on the way (of `heads_out`) count: a program that leaves them out, or rounds other values in their place, can miss the bound.
Values may be sent and summed in bfloat16 or wider, within the bound.
No kernel may reach another device: no remote copies, remote signals or barrier semaphores. Data moves between devices by JAX's collectives and lax.ppermute only.
A program may use at most 64 MiB of HBM per device.

```python
import math
import jax
import jax.numpy as jnp
import numpy as np
from jax import lax

D = 8192
H = 64
KVH = 8
HD = 128
SLOTS = 768
CAP = 3
MAXLEN = 256
R_DP = 64
REQUESTS = 256
N_ATTN = 64
N_DP = 4


def draw_kv_cache(key, part):
    shape = (N_DP, N_ATTN * SLOTS, 2, KVH, HD)
    base = jax.random.normal(jax.random.fold_in(key, 1), shape, jnp.float32)
    return base.astype(jnp.bfloat16)


def steps_of(stream_key, shape, shards, least, top_value):
    loudness, own = 1.0, jax.random.fold_in(stream_key, 6)
    for position, parts in shards:
        draws = jnp.exp(jax.random.uniform(jax.random.fold_in(own, position), (parts,), jnp.float32, least / len(shards), top_value / len(shards)))
        loudness = loudness * jnp.repeat(draws, shape[position] // parts).reshape([-1 if axis == position else 1 for axis in range(len(shape))])
    return loudness


def profile(number_of, total, bound, lean):
    portions = [(1 << 20) // math.isqrt(standing ** lean) + 1 for standing in range(2, number_of + 1)]
    rest, holding = total - bound - (number_of - 1), [1] * (number_of - 1)
    while rest > 0:
        candidates = [i for i in range(number_of - 1) if holding[i] < bound]
        whole, remaining = sum([portions[i] for i in candidates]), rest
        for i in candidates:
            extra = min(bound - holding[i], max(1, remaining * portions[i] // whole), rest)
            holding[i] = holding[i] + extra
            rest = rest - extra
    return np.array([bound] + holding)


def uneven(stream_key, count, total, limit, skew):
    if count == 2:
        one = jax.random.randint(stream_key, (), max(1, total - limit), min(limit, total - 1) + 1)
        return jnp.stack([one, total - one])
    sizes = jnp.asarray(profile(count, total, limit, skew), jnp.int32)
    twos = (count - 1) // 2
    donor, receiver = sizes[1:1 + 2 * twos:2], sizes[2:2 + 2 * twos:2]
    slack = jnp.minimum(donor - 1, limit - receiver)
    passed = jax.random.randint(jax.random.fold_in(stream_key, 1), (twos,), 0, 1 << 20) % (slack + 1)
    sizes = sizes.at[1:1 + 2 * twos:2].set(donor - passed).at[2:2 + 2 * twos:2].set(receiver + passed)
    return sizes[jax.random.permutation(jax.random.fold_in(stream_key, 2), count)]


def routed_block(stream_key, own, number, rows, count, top, most, slope):
    sequence = jax.random.permutation(stream_key, count)
    packed, ordinary = shares(count, rows * top, most, slope, True), shares(count, rows * top, most, slope, False)
    places = jnp.arange(count)

    def named(tallies, rotation):
        used = int((tallies > 0).sum())
        fixed = max(1, used // 4)
        shifted = fixed + (places - fixed + rotation * (used - fixed)) % max(1, count - fixed)
        return jnp.zeros((count,), jnp.int32).at[sequence[jnp.where(places < fixed, places, shifted)]].set(jnp.asarray(tallies, jnp.int32))

    tallies = jnp.where(number % 4 == 0, named(packed, number // 4), named(ordinary, number - number // 4 - 1))
    mixed = jax.random.permutation(jax.random.fold_in(own, 3), count)
    source_of, sink = mixed[0:count // 2 * 2:2], mixed[1:count // 2 * 2:2]
    margin = jnp.minimum(tallies[source_of] - 1, most - tallies[sink]) // 2
    margin = jnp.where((source_of == sequence[0]) | (sink == sequence[0]) | (tallies[sink] == 0), 0, jnp.maximum(margin, 0))
    shifted = jax.random.randint(jax.random.fold_in(own, 4), (count // 2,), 0, 1 << 20) % (margin + 1)
    tallies = tallies.at[source_of].add(-shifted).at[sink].add(shifted)
    items = jnp.searchsorted(jnp.cumsum(tallies), jnp.arange(rows * top), side="right").astype(jnp.int32)
    grid = items.reshape(top, rows).T
    grid = grid[jax.random.permutation(jax.random.fold_in(own, 1), rows)]
    rotation = jax.random.randint(jax.random.fold_in(own, 2), (rows, 1), 0, top)
    return jnp.take_along_axis(grid, (jnp.arange(top)[None, :] + rotation) % top, axis=1)


def shares(count, total, reach, slope, full):
    portions = [(1 << 20) // math.isqrt(standing ** slope) + 1 for standing in range(1, count + 1)]
    largest = reach if full else min(reach, max(-(-total // count), total * portions[0] // sum(portions)))
    least = 1 if total - largest >= count - 1 else 0
    counts, surplus = [largest] + [least] * (count - 1), total - largest - least * (count - 1)
    while surplus > 0:
        candidates = [i for i in range(1, count) if counts[i] < largest] or [i for i in range(1, count) if counts[i] < reach]
        whole, left = sum([portions[i] for i in candidates]), surplus
        for i in candidates:
            extra = min(reach - counts[i], max(1, left * portions[i] // whole), surplus)
            counts[i] = counts[i] + extra
            surplus = surplus - extra
    return np.array(counts)


def noise(key, shape, scale, most, cuts=(), held_as=jnp.bfloat16):
    drawn = scale * jax.random.normal(key, shape, jnp.float32)
    if cuts:
        drawn = drawn * steps_of(key, shape, cuts, -0.22, 0.18)
    return jnp.clip(drawn, -most, most).astype(held_as)


def setup_inputs(seed: int = 0) -> dict:
    key_list = jax.random.split(jax.random.key(seed), 8)
    hidden_state = noise(key_list[0], (REQUESTS, D), 1.0, 6.0, ((0, 4), (1, 64)))
    w_query = noise(key_list[1], (D, H * HD), D ** -0.5, 0.0625, ((0, 64), (1, 2)))
    w_keyval = noise(key_list[2], (D, 2, KVH * HD), D ** -0.5, 0.0625, ((0, 64), (2, 2)))
    w_output = noise(key_list[3], (H * HD, D), (H * HD) ** -0.5, 0.0625, ((0, 2), (1, 64)))
    kv_cache = draw_kv_cache(jax.random.fold_in(key_list[7], 71), 0)
    lengths = jax.vmap(lambda own: uneven(own, R_DP, R_DP * MAXLEN // 2, MAXLEN, 2))(jax.random.split(key_list[5], N_DP)).reshape((N_DP, R_DP)).astype(jnp.int32)
    owner_of_keys = jax.random.split(jax.random.fold_in(key_list[6], 1), N_DP * R_DP // R_DP)
    owner_of_turns = jax.random.permutation(jax.random.fold_in(key_list[6], 3), N_DP * R_DP // R_DP)
    owner_of = jax.vmap(lambda own, number: routed_block(jax.random.fold_in(key_list[6], 2), own, number, R_DP, N_ATTN, 1, CAP, 2))(owner_of_keys, owner_of_turns).reshape((N_DP, R_DP, 1))
    return {"hidden_state": hidden_state, "w_query": w_query, "w_keyval": w_keyval, "w_output": w_output, "kv_cache": kv_cache, "lengths": lengths, "owner_of": owner_of}


ROPE_BASE = 500000.0

def rotate_pairs(vectors, positions):
    half_dim = vectors.shape[-1] // 2
    steps_f = jnp.arange(half_dim).astype(jnp.float32) * (2.0 / vectors.shape[-1])
    inv_freq = jnp.exp(-math.log(ROPE_BASE) * steps_f)
    angles = positions[:, None] * inv_freq[None, :]
    cosine = jnp.cos(angles)[:, None, :]
    sine_part = jnp.sin(angles)[:, None, :]
    front_half = vectors[..., :half_dim]
    back_half = vectors[..., half_dim:]
    return jnp.concatenate([front_half * cosine - back_half * sine_part, back_half * cosine + front_half * sine_part], axis=-1)

def reference(hidden_state, w_query, w_keyval, w_output, kv_cache, lengths, owner_of):
    total = hidden_state.shape[0]
    group_size = H // KVH
    score_scale = 1.0 / math.sqrt(HD)
    query_full = jnp.dot(hidden_state, w_query, preferred_element_type=jnp.float32).reshape(total, H, HD)
    keyval_full = jnp.dot(hidden_state, w_keyval.reshape(D, 2 * KVH * HD), preferred_element_type=jnp.float32).reshape(total, 2, KVH, HD)
    req_lens = lengths.reshape(total).astype(jnp.int32)
    positions = req_lens.astype(jnp.float32)
    queries = rotate_pairs(query_full, positions).astype(jnp.bfloat16)
    new_keys = rotate_pairs(keyval_full[:, 0], positions).astype(jnp.bfloat16)
    new_vals = keyval_full[:, 1].astype(jnp.bfloat16)
    owners = owner_of.reshape(N_DP, R_DP).astype(jnp.int32)
    req_order = jnp.arange(R_DP).astype(jnp.int32)
    earlier = req_order[None, :] < req_order[:, None]
    same_owner = owners[:, :, None] == owners[:, None, :]
    starts = lax.optimization_barrier(jnp.sum(jnp.where(same_owner & earlier[None], lengths.astype(jnp.int32)[:, None, :], 0), axis=2)).astype(jnp.int32).reshape(total)
    group_ids = (jnp.arange(total) // R_DP).astype(jnp.int32)
    own_flat = owners.reshape(total)
    slot_pos = jnp.arange(SLOTS).astype(jnp.int32)
    zero_idx = jnp.zeros((), jnp.int32)

    def attend_one(item):
        query_row, new_key, new_val, group_idx, owner_idx, first_slot, length = item
        block = lax.dynamic_slice(kv_cache, (group_idx, owner_idx * SLOTS, zero_idx, zero_idx, zero_idx), (1, SLOTS, 2, KVH, HD))[0]
        cache_keys = block[:, 0].astype(jnp.float32)
        cache_vals = block[:, 1].astype(jnp.float32)
        grouped = query_row.astype(jnp.float32).reshape(KVH, group_size, HD)
        scores = jnp.einsum('kgd,skd->kgs', grouped, cache_keys) * score_scale
        own_score = jnp.einsum('kgd,kd->kg', grouped, new_key.astype(jnp.float32)) * score_scale
        live = (slot_pos >= first_slot) & (slot_pos < first_slot + length)
        row_max = jnp.maximum(lax.optimization_barrier(jnp.max(jnp.where(live, scores, -jnp.inf), axis=-1)), own_score)
        weights = jnp.where(live, jnp.exp(scores - row_max[..., None]), 0.0)
        own_weight = jnp.exp(own_score - row_max)
        total_weight = lax.optimization_barrier(jnp.sum(weights, axis=-1)) + own_weight
        probs = (weights / total_weight[..., None]).astype(jnp.bfloat16)
        own_prob = (own_weight / total_weight).astype(jnp.bfloat16)
        mixed = jnp.einsum('kgs,skd->kgd', probs.astype(jnp.float32), cache_vals)
        mixed = mixed + own_prob.astype(jnp.float32)[..., None] * new_val.astype(jnp.float32)[:, None, :]
        return mixed.reshape(H * HD).astype(jnp.bfloat16)
    heads_out = lax.map(attend_one, (queries, new_keys, new_vals, group_ids, own_flat, starts, req_lens))
    return jnp.dot(heads_out, w_output, preferred_element_type=jnp.float32).astype(jnp.bfloat16)
```

```python
import math

import jax
import jax.numpy as jnp
from jax import lax
from jax.sharding import Mesh
from jax.sharding import PartitionSpec as P

HD = 128
CAP = 3
Y_PARTS = 4


ROPE_BASE = 500000.0


def rotate_pairs(vectors, positions):
    half_dim = vectors.shape[-1] // 2
    steps_f = jnp.arange(half_dim).astype(jnp.float32) * (2.0 / vectors.shape[-1])
    inv_freq = jnp.exp(-math.log(ROPE_BASE) * steps_f)
    angles = positions[:, None] * inv_freq[None, :]
    cosine = jnp.cos(angles)[:, None, :]
    sine_part = jnp.sin(angles)[:, None, :]
    front_half = vectors[..., :half_dim]
    back_half = vectors[..., half_dim:]
    return jnp.concatenate(
        [front_half * cosine - back_half * sine_part, back_half * cosine + front_half * sine_part],
        axis=-1,
    )


def gather_rows(rows, n_y, n_z):
    stage = lax.all_to_all(jnp.tile(rows[None], (n_z, 1, 1)), "az", 0, 0, tiled=True)
    stage = lax.all_to_all(jnp.tile(stage[None], (n_y, 1, 1, 1)), "ay", 0, 0, tiled=True)
    return stage.reshape((n_y * n_z * rows.shape[0],) + rows.shape[1:])


def local(hidden_state, w_query, w_keyval, w_output, kv_cache, lengths, owner_of, n_y, n_z):
    rows_group = hidden_state.shape[0]
    width_loc = hidden_state.shape[1]
    my_index = lax.axis_index("ay") * n_z + lax.axis_index("az")
    heads_loc = w_query.shape[1] // HD
    kv_loc = w_keyval.shape[2] // HD
    group_size = heads_loc // kv_loc
    q_cols = heads_loc * HD
    kv_cols = kv_loc * HD
    score_scale = 1.0 / math.sqrt(HD)
    query_part = jnp.dot(hidden_state, w_query, preferred_element_type=jnp.float32)
    keyval_part = jnp.dot(
        hidden_state,
        w_keyval.reshape(width_loc, 2 * kv_cols),
        preferred_element_type=jnp.float32,
    )
    both = jnp.concatenate([query_part, keyval_part], axis=1)
    cols = both.shape[1]
    per_y = rows_group // n_y
    part = lax.all_to_all(both.reshape(n_y, per_y, cols), "ay", 0, 0, tiled=True).sum(0)
    part = lax.all_to_all(part.reshape(n_z, per_y // n_z, cols), "az", 0, 0, tiled=True).sum(0)
    owners = owner_of.reshape(rows_group)
    req_lens = lengths.reshape(rows_group)
    mine_pos = lax.dynamic_slice(req_lens, (my_index,), (1,)).astype(jnp.float32)
    q_rot = rotate_pairs(part[:, :q_cols].reshape(1, heads_loc, HD), mine_pos).astype(jnp.bfloat16)
    k_rot = rotate_pairs(part[:, q_cols : q_cols + kv_cols].reshape(1, kv_loc, HD), mine_pos).astype(
        jnp.bfloat16
    )
    v_new = part[:, q_cols + kv_cols :].astype(jnp.bfloat16)
    row_bf = jnp.concatenate(
        [q_rot.reshape(1, q_cols), k_rot.reshape(1, kv_cols), v_new.reshape(1, kv_cols)], axis=1
    )
    all_rows = gather_rows(row_bf, n_y, n_z)
    query_rows = all_rows[:, :q_cols]
    keyval_rows = all_rows[:, q_cols:]
    req_order = jnp.arange(rows_group, dtype=jnp.int32)
    same_owner = owners[:, None] == owners[None, :]
    earlier = req_order[None, :] < req_order[:, None]
    before_mine = same_owner & earlier
    starts = jnp.sum(jnp.where(before_mine, req_lens[None, :], 0), axis=1)
    slot_rank = jnp.sum(before_mine.astype(jnp.int32), axis=1)
    slot_hit = (owners[None, :] == my_index) & (
        slot_rank[None, :] == jnp.arange(CAP, dtype=jnp.int32)[:, None]
    )
    chosen = jnp.sum(jnp.where(slot_hit, req_order[None, :], 0), axis=1)
    present = jnp.any(slot_hit, axis=1)
    my_start = jnp.take(starts, chosen)
    my_len = jnp.where(present, jnp.take(req_lens, chosen), 0)
    query_mine = jnp.take(query_rows, chosen, axis=0)
    keyval_mine = jnp.take(keyval_rows, chosen, axis=0).reshape(CAP, 2, kv_loc, HD)
    cache_local = kv_cache[0]
    grouped = query_mine.reshape(CAP, kv_loc, group_size, HD)
    scores = (
        jnp.einsum("ckgd,skd->ckgs", grouped, cache_local[:, 0], preferred_element_type=jnp.float32)
        * score_scale
    )
    own_score = (
        jnp.einsum("ckgd,ckd->ckg", grouped, keyval_mine[:, 0], preferred_element_type=jnp.float32)
        * score_scale
    )
    slot_pos = jnp.arange(cache_local.shape[0], dtype=jnp.int32)
    live = (slot_pos[None, :] >= my_start[:, None]) & (
        slot_pos[None, :] < (my_start + my_len)[:, None]
    )
    live = live[:, None, None, :]
    row_max = jnp.maximum(jnp.max(jnp.where(live, scores, -jnp.inf), axis=-1), own_score)
    weights = jnp.where(live, jnp.exp(scores - row_max[..., None]), 0.0)
    own_weight = jnp.exp(own_score - row_max)
    total_weight = jnp.sum(weights, axis=-1) + own_weight
    probs = (weights / total_weight[..., None]).astype(jnp.bfloat16)
    own_prob = (own_weight / total_weight).astype(jnp.bfloat16)
    mixed = jnp.einsum(
        "ckgs,skd->ckgd", probs, cache_local[:, 1], preferred_element_type=jnp.float32
    )
    mixed = (
        mixed
        + own_prob.astype(jnp.float32)[..., None]
        * keyval_mine[:, 1].astype(jnp.float32)[:, :, None, :]
    )
    out_slots = mixed.reshape(CAP, heads_loc * HD).astype(jnp.bfloat16)
    gathered = gather_rows(out_slots, n_y, n_z)
    heads_out = jnp.take(gathered, owners * CAP + slot_rank, axis=0)
    out_part = jnp.dot(heads_out, w_output, preferred_element_type=jnp.float32)
    out_total = lax.psum(out_part, "tensor")
    return out_total.astype(jnp.bfloat16)


def solution(mesh):
    n_attn = mesh.shape["attn"]
    n_y = Y_PARTS if n_attn % Y_PARTS == 0 else 1
    n_z = n_attn // n_y
    devs = mesh.devices
    sub = Mesh(devs.reshape((n_y, n_z) + devs.shape[1:]), ("ay", "az") + tuple(mesh.axis_names[1:]))
    A = ("ay", "az")
    placed = (
        P("dp", A),
        P(A, "tensor"),
        P(A, None, "tensor"),
        P("tensor", A),
        P("dp", A, None, "tensor", None),
        P("dp", None),
        P("dp", None, None),
    )

    def body(*args):
        return local(*args, n_y=n_y, n_z=n_z)

    return jax.shard_map(body, mesh=sub, in_specs=placed, out_specs=P("dp", A), check_vma=False)
```

```python
import math

import jax
import jax.numpy as jnp
from jax import lax
from jax.sharding import Mesh
from jax.sharding import PartitionSpec as P

HD = 128
CAP = 3
Y_PARTS = 4


ROPE_BASE = 500000.0


def rotate_pairs(vectors, positions):
    half_dim = vectors.shape[-1] // 2
    steps_f = jnp.arange(half_dim).astype(jnp.float32) * (2.0 / vectors.shape[-1])
    inv_freq = jnp.exp(-math.log(ROPE_BASE) * steps_f)
    angles = positions[:, None] * inv_freq[None, :]
    cosine = jnp.cos(angles)[:, None, :]
    sine_part = jnp.sin(angles)[:, None, :]
    front_half = vectors[..., :half_dim]
    back_half = vectors[..., half_dim:]
    return jnp.concatenate(
        [front_half * cosine - back_half * sine_part, back_half * cosine + front_half * sine_part],
        axis=-1,
    )


def gather_rows(rows, n_y, n_z):
    stage = lax.all_to_all(jnp.tile(rows[None], (n_z, 1, 1)), "az", 0, 0, tiled=True)
    stage = lax.all_to_all(jnp.tile(stage[None], (n_y, 1, 1, 1)), "ay", 0, 0, tiled=True)
    return stage.reshape((n_y * n_z * rows.shape[0],) + rows.shape[1:])


def local(hidden_state, w_query, w_keyval, w_output, kv_cache, lengths, owner_of, n_y, n_z):
    rows_group = hidden_state.shape[0]
    width_loc = hidden_state.shape[1]
    my_index = lax.axis_index("ay") * n_z + lax.axis_index("az")
    heads_loc = w_query.shape[1] // HD
    kv_loc = w_keyval.shape[2] // HD
    group_size = heads_loc // kv_loc
    q_cols = heads_loc * HD
    kv_cols = kv_loc * HD
    score_scale = 1.0 / math.sqrt(HD)
    query_part = jnp.dot(hidden_state, w_query, preferred_element_type=jnp.float32)
    keyval_part = jnp.dot(
        hidden_state,
        w_keyval.reshape(width_loc, 2 * kv_cols),
        preferred_element_type=jnp.float32,
    )
    both = jnp.concatenate([query_part, keyval_part], axis=1)
    cols = both.shape[1]
    per_y = rows_group // n_y
    part = lax.all_to_all(both.reshape(n_y, per_y, cols), "ay", 0, 0, tiled=True).sum(0)
    part = lax.all_to_all(part.reshape(n_z, cols // HD, HD), "az", 0, 0, tiled=True).sum(0)
    part = part.reshape(1, cols)
    owners = owner_of.reshape(rows_group)
    req_lens = lengths.reshape(rows_group)
    mine_pos = lax.dynamic_slice(req_lens, (my_index,), (1,)).astype(jnp.float32)
    q_rot = rotate_pairs(part[:, :q_cols].reshape(1, heads_loc, HD), mine_pos).astype(jnp.bfloat16)
    k_rot = rotate_pairs(part[:, q_cols : q_cols + kv_cols].reshape(1, kv_loc, HD), mine_pos).astype(
        jnp.bfloat16
    )
    v_new = part[:, q_cols + kv_cols :].astype(jnp.bfloat16)
    row_bf = jnp.concatenate(
        [q_rot.reshape(1, q_cols), k_rot.reshape(1, kv_cols), v_new.reshape(1, kv_cols)], axis=1
    )
    all_rows = gather_rows(row_bf.reshape(cols // HD, HD), n_y, n_z).reshape(-1, cols)
    query_rows = all_rows[:, :q_cols]
    keyval_rows = all_rows[:, q_cols:]
    req_order = jnp.arange(rows_group, dtype=jnp.int32)
    same_owner = owners[:, None] == owners[None, :]
    earlier = req_order[None, :] < req_order[:, None]
    before_mine = same_owner & earlier
    starts = jnp.sum(jnp.where(before_mine, req_lens[None, :], 0), axis=1)
    slot_rank = jnp.sum(before_mine.astype(jnp.int32), axis=1)
    slot_hit = (owners[None, :] == my_index) & (
        slot_rank[None, :] == jnp.arange(CAP, dtype=jnp.int32)[:, None]
    )
    chosen = jnp.sum(jnp.where(slot_hit, req_order[None, :], 0), axis=1)
    present = jnp.any(slot_hit, axis=1)
    my_start = jnp.take(starts, chosen)
    my_len = jnp.where(present, jnp.take(req_lens, chosen), 0)
    query_mine = jnp.take(query_rows, chosen, axis=0)
    keyval_mine = jnp.take(keyval_rows, chosen, axis=0).reshape(CAP, 2, kv_loc, HD)
    cache_local = kv_cache[0]
    grouped = query_mine.reshape(CAP, kv_loc, group_size, HD)
    scores = (
        jnp.einsum("ckgd,skd->ckgs", grouped, cache_local[:, 0], preferred_element_type=jnp.float32)
        * score_scale
    )
    own_score = (
        jnp.einsum("ckgd,ckd->ckg", grouped, keyval_mine[:, 0], preferred_element_type=jnp.float32)
        * score_scale
    )
    slot_pos = jnp.arange(cache_local.shape[0], dtype=jnp.int32)
    live = (slot_pos[None, :] >= my_start[:, None]) & (
        slot_pos[None, :] < (my_start + my_len)[:, None]
    )
    live = live[:, None, None, :]
    row_max = jnp.maximum(jnp.max(jnp.where(live, scores, -jnp.inf), axis=-1), own_score)
    weights = jnp.where(live, jnp.exp(scores - row_max[..., None]), 0.0)
    own_weight = jnp.exp(own_score - row_max)
    total_weight = jnp.sum(weights, axis=-1) + own_weight
    probs = (weights / total_weight[..., None]).astype(jnp.bfloat16)
    own_prob = (own_weight / total_weight).astype(jnp.bfloat16)
    mixed = jnp.einsum(
        "ckgs,skd->ckgd", probs, cache_local[:, 1], preferred_element_type=jnp.float32
    )
    mixed = (
        mixed
        + own_prob.astype(jnp.float32)[..., None]
        * keyval_mine[:, 1].astype(jnp.float32)[:, :, None, :]
    )
    out_slots = mixed.reshape(CAP, heads_loc * HD).astype(jnp.bfloat16)
    lanes = out_slots.size // 16
    gathered = gather_rows(out_slots.reshape(16, lanes), n_y, n_z)
    gathered = gathered.reshape(-1, heads_loc * HD)
    heads_out = jnp.take(gathered, owners * CAP + slot_rank, axis=0)
    out_part = jnp.dot(heads_out, w_output, preferred_element_type=jnp.float32)
    out_total = lax.psum(out_part, "tensor")
    return out_total.astype(jnp.bfloat16)


def solution(mesh):
    n_attn = mesh.shape["attn"]
    n_y = Y_PARTS if n_attn % Y_PARTS == 0 else 1
    n_z = n_attn // n_y
    devs = mesh.devices
    sub = Mesh(devs.reshape((n_y, n_z) + devs.shape[1:]), ("ay", "az") + tuple(mesh.axis_names[1:]))
    A = ("ay", "az")
    placed = (
        P("dp", A),
        P(A, "tensor"),
        P(A, None, "tensor"),
        P("tensor", A),
        P("dp", A, None, "tensor", None),
        P("dp", None),
        P("dp", None, None),
    )

    def body(*args):
        return local(*args, n_y=n_y, n_z=n_z)

    return jax.shard_map(body, mesh=sub, in_specs=placed, out_specs=P("dp", A), check_vma=False)
```

```python
import math

import jax
import jax.numpy as jnp
from jax import lax
from jax.sharding import Mesh
from jax.sharding import PartitionSpec as P

HD = 128
CAP = 3
Y_PARTS = 4


ROPE_BASE = 500000.0


def rotate_pairs(vectors, positions):
    half_dim = vectors.shape[-1] // 2
    steps_f = jnp.arange(half_dim).astype(jnp.float32) * (2.0 / vectors.shape[-1])
    inv_freq = jnp.exp(-math.log(ROPE_BASE) * steps_f)
    angles = positions[:, None] * inv_freq[None, :]
    cosine = jnp.cos(angles)[:, None, :]
    sine_part = jnp.sin(angles)[:, None, :]
    front_half = vectors[..., :half_dim]
    back_half = vectors[..., half_dim:]
    return jnp.concatenate(
        [front_half * cosine - back_half * sine_part, back_half * cosine + front_half * sine_part],
        axis=-1,
    )


def gather_rows(rows, n_y, n_z):
    stage = lax.all_to_all(jnp.tile(rows[None], (n_z, 1, 1)), "az", 0, 0, tiled=True)
    stage = lax.all_to_all(jnp.tile(stage[None], (n_y, 1, 1, 1)), "ay", 0, 0, tiled=True)
    return stage.reshape((n_y * n_z * rows.shape[0],) + rows.shape[1:])


def local(hidden_state, w_query, w_keyval, w_output, kv_cache, lengths, owner_of, n_y, n_z):
    rows_group = hidden_state.shape[0]
    width_loc = hidden_state.shape[1]
    my_index = lax.axis_index("ay") * n_z + lax.axis_index("az")
    heads_loc = w_query.shape[1] // HD
    kv_loc = w_keyval.shape[2] // HD
    group_size = heads_loc // kv_loc
    q_cols = heads_loc * HD
    kv_cols = kv_loc * HD
    score_scale = 1.0 / math.sqrt(HD)
    query_part = jnp.dot(hidden_state, w_query, preferred_element_type=jnp.float32)
    keyval_part = jnp.dot(
        hidden_state,
        w_keyval.reshape(width_loc, 2 * kv_cols),
        preferred_element_type=jnp.float32,
    )
    both = jnp.concatenate([query_part, keyval_part], axis=1)
    cols = both.shape[1]
    per_y = rows_group // n_y
    part = lax.all_to_all(both.reshape(n_y, per_y, cols), "ay", 0, 0, tiled=True).sum(0)
    part = lax.all_to_all(part.reshape(n_z, cols // HD, HD), "az", 0, 0, tiled=True).sum(0)
    part = part.reshape(1, cols)
    owners = owner_of.reshape(rows_group)
    req_lens = lengths.reshape(rows_group)
    mine_pos = lax.dynamic_slice(req_lens, (my_index,), (1,)).astype(jnp.float32)
    q_rot = rotate_pairs(part[:, :q_cols].reshape(1, heads_loc, HD), mine_pos).astype(jnp.bfloat16)
    k_rot = rotate_pairs(part[:, q_cols : q_cols + kv_cols].reshape(1, kv_loc, HD), mine_pos).astype(
        jnp.bfloat16
    )
    v_new = part[:, q_cols + kv_cols :].astype(jnp.bfloat16)
    row_bf = jnp.concatenate(
        [q_rot.reshape(1, q_cols), k_rot.reshape(1, kv_cols), v_new.reshape(1, kv_cols)], axis=1
    )
    all_rows = gather_rows(row_bf.reshape(cols // HD, HD), n_y, n_z).reshape(-1, cols)
    query_rows = all_rows[:, :q_cols]
    keyval_rows = all_rows[:, q_cols:]
    req_order = jnp.arange(rows_group, dtype=jnp.int32)
    same_owner = owners[:, None] == owners[None, :]
    earlier = req_order[None, :] < req_order[:, None]
    before_mine = same_owner & earlier
    starts = jnp.sum(jnp.where(before_mine, req_lens[None, :], 0), axis=1)
    slot_rank = jnp.sum(before_mine.astype(jnp.int32), axis=1)
    slot_hit = (owners[None, :] == my_index) & (
        slot_rank[None, :] == jnp.arange(CAP, dtype=jnp.int32)[:, None]
    )
    chosen = jnp.sum(jnp.where(slot_hit, req_order[None, :], 0), axis=1)
    present = jnp.any(slot_hit, axis=1)
    my_start = jnp.take(starts, chosen)
    my_len = jnp.where(present, jnp.take(req_lens, chosen), 0)
    query_mine = jnp.take(query_rows, chosen, axis=0)
    keyval_mine = jnp.take(keyval_rows, chosen, axis=0).reshape(CAP, 2, kv_loc, HD)
    cache_local = kv_cache[0]
    grouped = query_mine.reshape(CAP, kv_loc, group_size, HD)
    scores = (
        jnp.einsum("ckgd,skd->ckgs", grouped, cache_local[:, 0], preferred_element_type=jnp.float32)
        * score_scale
    )
    own_score = (
        jnp.einsum("ckgd,ckd->ckg", grouped, keyval_mine[:, 0], preferred_element_type=jnp.float32)
        * score_scale
    )
    slot_pos = jnp.arange(cache_local.shape[0], dtype=jnp.int32)
    live = (slot_pos[None, :] >= my_start[:, None]) & (
        slot_pos[None, :] < (my_start + my_len)[:, None]
    )
    live = live[:, None, None, :]
    row_max = jnp.maximum(jnp.max(jnp.where(live, scores, -jnp.inf), axis=-1), own_score)
    weights = jnp.where(live, jnp.exp(scores - row_max[..., None]), 0.0)
    own_weight = jnp.exp(own_score - row_max)
    total_weight = jnp.sum(weights, axis=-1) + own_weight
    probs = (weights / total_weight[..., None]).astype(jnp.bfloat16)
    own_prob = (own_weight / total_weight).astype(jnp.bfloat16)
    mixed = jnp.einsum(
        "ckgs,skd->ckgd", probs, cache_local[:, 1], preferred_element_type=jnp.float32
    )
    mixed = (
        mixed
        + own_prob.astype(jnp.float32)[..., None]
        * keyval_mine[:, 1].astype(jnp.float32)[:, :, None, :]
    )
    out_slots = mixed.reshape(CAP, heads_loc * HD).astype(jnp.bfloat16)
    slot_rows = heads_loc * HD // 256
    gathered = gather_rows(out_slots.reshape(CAP * slot_rows, 256), n_y, n_z)
    gathered = gathered.reshape(-1, slot_rows, 256)
    heads_out = jnp.take(gathered, owners * CAP + slot_rank, axis=0).reshape(rows_group, -1)
    out_part = jnp.dot(heads_out, w_output, preferred_element_type=jnp.float32)
    out_total = out_part + lax.ppermute(out_part, "tensor", [(0, 1), (1, 0)])
    return out_total.astype(jnp.bfloat16)


def solution(mesh):
    n_attn = mesh.shape["attn"]
    n_y = Y_PARTS if n_attn % Y_PARTS == 0 else 1
    n_z = n_attn // n_y
    devs = mesh.devices
    sub = Mesh(devs.reshape((n_y, n_z) + devs.shape[1:]), ("ay", "az") + tuple(mesh.axis_names[1:]))
    A = ("ay", "az")
    placed = (
        P("dp", A),
        P(A, "tensor"),
        P(A, None, "tensor"),
        P("tensor", A),
        P("dp", A, None, "tensor", None),
        P("dp", None),
        P("dp", None, None),
    )

    def body(*args):
        return local(*args, n_y=n_y, n_z=n_z)

    return jax.shard_map(body, mesh=sub, in_specs=placed, out_specs=P("dp", A), check_vma=False)
```

```python
import math

import jax
import jax.numpy as jnp
from jax import lax
from jax.sharding import Mesh
from jax.sharding import PartitionSpec as P

HD = 128
CAP = 3
Y_PARTS = 4


ROPE_BASE = 500000.0


def rotate_pairs(vectors, positions):
    half_dim = vectors.shape[-1] // 2
    steps_f = jnp.arange(half_dim).astype(jnp.float32) * (2.0 / vectors.shape[-1])
    inv_freq = jnp.exp(-math.log(ROPE_BASE) * steps_f)
    angles = positions[:, None] * inv_freq[None, :]
    cosine = jnp.cos(angles)[:, None, :]
    sine_part = jnp.sin(angles)[:, None, :]
    front_half = vectors[..., :half_dim]
    back_half = vectors[..., half_dim:]
    return jnp.concatenate(
        [front_half * cosine - back_half * sine_part, back_half * cosine + front_half * sine_part],
        axis=-1,
    )


def gather_rows(rows, n_y, n_z):
    stage = lax.all_to_all(jnp.tile(rows[None], (n_z, 1, 1)), "az", 0, 0, tiled=True)
    stage = lax.all_to_all(jnp.tile(stage[None], (n_y, 1, 1, 1)), "ay", 0, 0, tiled=True)
    return stage.reshape((n_y * n_z * rows.shape[0],) + rows.shape[1:])


def local(hidden_state, w_query, w_keyval, w_output, kv_cache, lengths, owner_of, n_y, n_z):
    rows_group = hidden_state.shape[0]
    width_loc = hidden_state.shape[1]
    my_index = lax.axis_index("ay") * n_z + lax.axis_index("az")
    heads_loc = w_query.shape[1] // HD
    kv_loc = w_keyval.shape[2] // HD
    group_size = heads_loc // kv_loc
    q_cols = heads_loc * HD
    kv_cols = kv_loc * HD
    score_scale = 1.0 / math.sqrt(HD)
    query_part = jnp.dot(hidden_state, w_query, preferred_element_type=jnp.float32)
    keyval_part = jnp.dot(
        hidden_state,
        w_keyval.reshape(width_loc, 2 * kv_cols),
        preferred_element_type=jnp.float32,
    )
    both = jnp.concatenate([query_part, keyval_part], axis=1)
    cols = both.shape[1]
    per_y = rows_group // n_y
    part = lax.all_to_all(both.reshape(n_y, per_y, cols), "ay", 0, 0, tiled=True).sum(0)
    part = lax.all_to_all(part.reshape(n_z, cols // HD, HD), "az", 0, 0, tiled=True).sum(0)
    part = part.reshape(1, cols)
    owners = owner_of.reshape(rows_group)
    req_lens = lengths.reshape(rows_group)
    mine_pos = lax.dynamic_slice(req_lens, (my_index,), (1,)).astype(jnp.float32)
    q_rot = rotate_pairs(part[:, :q_cols].reshape(1, heads_loc, HD), mine_pos).astype(jnp.bfloat16)
    k_rot = rotate_pairs(part[:, q_cols : q_cols + kv_cols].reshape(1, kv_loc, HD), mine_pos).astype(
        jnp.bfloat16
    )
    v_new = part[:, q_cols + kv_cols :].astype(jnp.bfloat16)
    row_bf = jnp.concatenate(
        [q_rot.reshape(1, q_cols), k_rot.reshape(1, kv_cols), v_new.reshape(1, kv_cols)], axis=1
    )
    tiles = cols // HD
    rows_z = lax.all_to_all(
        jnp.tile(row_bf.reshape(1, tiles, HD), (n_z, 1, 1)), "az", 0, 0, tiled=True
    ).reshape(n_z, cols)
    req_order = jnp.arange(rows_group, dtype=jnp.int32)
    same_owner = owners[:, None] == owners[None, :]
    earlier = req_order[None, :] < req_order[:, None]
    before_mine = same_owner & earlier
    starts = jnp.sum(jnp.where(before_mine, req_lens[None, :], 0), axis=1)
    slot_rank = jnp.sum(before_mine.astype(jnp.int32), axis=1)
    slot_hit = (owners[None, :] == my_index) & (
        slot_rank[None, :] == jnp.arange(CAP, dtype=jnp.int32)[:, None]
    )
    chosen = jnp.sum(jnp.where(slot_hit, req_order[None, :], 0), axis=1)
    present = jnp.any(slot_hit, axis=1)
    my_start = jnp.take(starts, chosen)
    my_len = jnp.where(present, jnp.take(req_lens, chosen), 0)
    dest_owner = jnp.arange(n_y, dtype=jnp.int32) * n_z + lax.axis_index("az")
    dest_hit = (owners[None, None, :] == dest_owner[:, None, None]) & (
        slot_rank[None, None, :] == jnp.arange(CAP, dtype=jnp.int32)[None, :, None]
    )
    dest_req = jnp.sum(jnp.where(dest_hit, req_order[None, None, :], 0), axis=2)
    send = jnp.take(rows_z, dest_req % n_z, axis=0).reshape(n_y, CAP * tiles, HD)
    recv = lax.all_to_all(send, "ay", 0, 0, tiled=True).reshape(n_y, CAP, cols)
    mine_rows = recv[chosen // n_z, jnp.arange(CAP)]
    query_mine = mine_rows[:, :q_cols]
    keyval_mine = mine_rows[:, q_cols:].reshape(CAP, 2, kv_loc, HD)
    cache_local = kv_cache[0]
    grouped = query_mine.reshape(CAP, kv_loc, group_size, HD)
    scores = (
        jnp.einsum("ckgd,skd->ckgs", grouped, cache_local[:, 0], preferred_element_type=jnp.float32)
        * score_scale
    )
    own_score = (
        jnp.einsum("ckgd,ckd->ckg", grouped, keyval_mine[:, 0], preferred_element_type=jnp.float32)
        * score_scale
    )
    slot_pos = jnp.arange(cache_local.shape[0], dtype=jnp.int32)
    live = (slot_pos[None, :] >= my_start[:, None]) & (
        slot_pos[None, :] < (my_start + my_len)[:, None]
    )
    live = live[:, None, None, :]
    row_max = jnp.maximum(jnp.max(jnp.where(live, scores, -jnp.inf), axis=-1), own_score)
    weights = jnp.where(live, jnp.exp(scores - row_max[..., None]), 0.0)
    own_weight = jnp.exp(own_score - row_max)
    total_weight = jnp.sum(weights, axis=-1) + own_weight
    probs = (weights / total_weight[..., None]).astype(jnp.bfloat16)
    own_prob = (own_weight / total_weight).astype(jnp.bfloat16)
    mixed = jnp.einsum(
        "ckgs,skd->ckgd", probs, cache_local[:, 1], preferred_element_type=jnp.float32
    )
    mixed = (
        mixed
        + own_prob.astype(jnp.float32)[..., None]
        * keyval_mine[:, 1].astype(jnp.float32)[:, :, None, :]
    )
    out_slots = mixed.reshape(CAP, heads_loc * HD).astype(jnp.bfloat16)
    slot_rows = heads_loc * HD // 256
    gathered = gather_rows(out_slots.reshape(CAP * slot_rows, 256), n_y, n_z)
    gathered = gathered.reshape(-1, slot_rows, 256)
    heads_out = jnp.take(gathered, owners * CAP + slot_rank, axis=0).reshape(rows_group, -1)
    out_part = jnp.dot(heads_out, w_output, preferred_element_type=jnp.float32)
    out_total = out_part + lax.ppermute(out_part, "tensor", [(0, 1), (1, 0)])
    return out_total.astype(jnp.bfloat16)


def solution(mesh):
    n_attn = mesh.shape["attn"]
    n_y = Y_PARTS if n_attn % Y_PARTS == 0 else 1
    n_z = n_attn // n_y
    devs = mesh.devices
    sub = Mesh(devs.reshape((n_y, n_z) + devs.shape[1:]), ("ay", "az") + tuple(mesh.axis_names[1:]))
    A = ("ay", "az")
    placed = (
        P("dp", A),
        P(A, "tensor"),
        P(A, None, "tensor"),
        P("tensor", A),
        P("dp", A, None, "tensor", None),
        P("dp", None),
        P("dp", None, None),
    )

    def body(*args):
        return local(*args, n_y=n_y, n_z=n_z)

    return jax.shard_map(body, mesh=sub, in_specs=placed, out_specs=P("dp", A), check_vma=False)
```
